128 devices in a mesh: col: 8 (over y, z_hi), pair: 16 (over x, z_lo, core).
Axes of the slice: x: 4, y: 4, z: 4 (z_hi: 2, z_lo: 2; z = z_hi * 2 + z_lo), core: 2. Of those that a mesh axis runs over, the one named last changes fastest.
Arguments:
- integrals: bfloat16 [512, 128, 128], P('pair', 'col'), may hold values from -6 to 6
- pno_energy: float32 [512, 128], P('pair'), may hold values from 0.5 to 4
- shift: float32 [512], P('pair'), may hold values from 0.5 to 2
- intersections: bfloat16 [512, 128, 128, 128], P('pair', 'col'), may hold values from -0.09375 to 0.09375
- links: int32 [512, 128], P('pair', 'col'), may hold values from 0 to 63
- counts: int32 [512], P('pair'), may hold values from 1 to 128, as said below
- column_of: int32 [512], P('pair'), may hold values from 0 to 63
Outputs:
- amplitudes: float32 [512, 128, 128], P('pair', 'col')
- pair_energy: float32 [512], P('pair')
The draws below stay inside these ranges and needn't reach their ends.
Inputs may be any that keep to these rules, and one draw needn't show every extreme that they name: Pair p couples through its first counts[p] slots; later slots are unused.
All inputs are finite; a program needn't handle non-finite values.
Results may differ from the reference program's by a relative error of at most 0.0012.
Values may be sent and summed in bfloat16 or wider, within the bound.
No kernel may reach another device: no remote copies, remote signals or barrier semaphores. Data moves between devices by JAX's collectives and lax.ppermute only.
A program may use at most 192 MiB of HBM per device.

```python
import math
import jax
import jax.numpy as jnp
from jax import lax

A = 128
SWEEPS = 3
PAIRS = 512
SLOTS = 128
NCOL = 64


def draw_counts(key, part):
    values = jax.random.randint(key, (PAIRS,), 1, SLOTS + 1).astype(jnp.int32)
    values = values.at[0].set(SLOTS)
    values = values.at[1].set(1)
    return values


def touch_ends(array, own_key, least, high):
    longest = array.shape.index(max(array.shape))
    spots = []
    for shift in (0, 1):
        where = [jax.random.randint(jax.random.fold_in(own_key, axis), (), 0, length) for axis, length in enumerate(array.shape)]
        where[longest] = (where[longest] + shift) % array.shape[longest]
        spots.append(tuple(where))
    return array.at[spots[0]].set(least).at[spots[1]].set(high)


def block_levels(stream_key, extent, shards, smallest, high):
    def one(position, parts):
        steps = jax.random.uniform(jax.random.fold_in(jax.random.fold_in(stream_key, 6), position), (parts,), jnp.float32, smallest / len(shards), high / len(shards))
        return jnp.repeat(jnp.exp(steps), extent[position] // parts).reshape((-1,) + (1,) * (len(extent) - position - 1))

    level = one(*shards[0])
    for cut in shards[1:]:
        level = level * one(*cut)
    return level


def scatter_about(key, dims, deviation, reach, shards=(), held_as=jnp.bfloat16):
    loudness = block_levels(key, dims, shards, -0.22, 0.18) if shards else 1.0
    array = jax.random.normal(key, dims, jnp.float32) * deviation * loudness
    return jnp.minimum(jnp.maximum(array, -reach), reach).astype(held_as)


def setup_inputs(seed: int = 0) -> dict:
    key_list = jax.random.split(jax.random.key(seed), 8)
    return {
        "integrals": scatter_about(key_list[0], (PAIRS, A, A), 1.0, 6.0, ((0, 16), (1, 8))),
        "pno_energy": jnp.clip(jnp.exp(math.log(4.0) - 2.0794415 * jax.random.uniform(key_list[1], (PAIRS, A), jnp.float32) ** block_levels(key_list[1], (PAIRS, A), ((0, 16),), -0.2, 0.2)), 0.5, 4.0),
        "shift": jnp.clip(jnp.exp(math.log(2.0) - 1.3862944 * jax.random.uniform(key_list[2], (PAIRS,), jnp.float32) ** block_levels(key_list[2], (PAIRS,), ((0, 16),), -0.2, 0.2)), 0.5, 2.0),
        "intersections": scatter_about(key_list[3], (PAIRS, SLOTS, A, A), (32 * A) ** -0.5, 0.09375, ((0, 16), (1, 8))),
        "links": touch_ends(jax.random.randint(key_list[4], (PAIRS, SLOTS), 0, NCOL), jax.random.fold_in(key_list[4], 1), 0, NCOL - 1).astype(jnp.int32),
        "counts": draw_counts(jax.random.fold_in(key_list[7], 71), 0),
        "column_of": touch_ends(jax.random.randint(key_list[6], (PAIRS,), 0, NCOL), jax.random.fold_in(key_list[6], 1), 0, NCOL - 1).astype(jnp.int32),
    }


def reference(integrals, pno_energy, shift, intersections, links, counts, column_of):
    kfloat = integrals.astype(jnp.float32)
    denom = pno_energy[:, :, None] + pno_energy[:, None, :] + shift[:, None, None]
    amplitudes = -kfloat / denom
    live = (jnp.arange(SLOTS, dtype=jnp.int32)[None, :] < counts[:, None]).astype(jnp.float32)
    for sweep in range(SWEEPS):
        colamp = jax.ops.segment_sum(amplitudes, column_of, num_segments=NCOL).astype(jnp.bfloat16)

        def couple(items):
            tiles, chosen, weights = items
            tfloat = tiles.astype(jnp.float32)
            blocks = colamp[chosen].astype(jnp.float32)
            left = jnp.einsum("mab,mbc->mac", tfloat, blocks, precision=lax.Precision.HIGHEST).astype(jnp.bfloat16)
            left = lax.optimization_barrier(left).astype(jnp.float32)
            right = jnp.einsum("mac,mdc->mad", left, tfloat, precision=lax.Precision.HIGHEST)
            return jnp.sum(right * weights[:, None, None], axis=0)

        coupled = lax.map(couple, (intersections, links, live))
        amplitudes = -(kfloat + coupled) / denom
    pair_energy = jnp.sum(kfloat * amplitudes, axis=(1, 2))
    return amplitudes, pair_energy
```

```python
import functools

import jax
import jax.numpy as jnp
from jax import lax
from jax.experimental import pallas as pl
from jax.experimental.pallas import tpu as pltpu
from jax.sharding import PartitionSpec as P

COL_DEV = 8
SWEEPS = 3
PAIR_BLOCK = 4


def couple_kernel(slot_dev, links_ref, nlive_ref, tiles_ref, colamp_ref, out_ref):
    step = pl.program_id(0)
    width = tiles_ref.shape[-1]
    for q in range(PAIR_BLOCK):
        pair = step * PAIR_BLOCK + q
        live = nlive_ref[pair]
        acc = jnp.zeros((width, width), jnp.float32)
        for m in range(slot_dev):
            tile = tiles_ref[q, m]
            block = colamp_ref[links_ref[pair * slot_dev + m]]
            left = jnp.dot(tile, block, preferred_element_type=jnp.float32)
            left = jnp.where(m < live, left, 0.0).astype(jnp.bfloat16)
            acc = acc + lax.dot_general(
                left, tile, (((1,), (1,)), ((), ())), preferred_element_type=jnp.float32
            )
        out_ref[:, q] = acc.reshape(out_ref.shape[0], out_ref.shape[2], width)


def couple(tiles, colamp, links, nlive, col_size):
    pair_dev, slot_dev, width, _ = tiles.shape
    ncol = colamp.shape[0]
    rows = width // col_size
    grid_spec = pltpu.PrefetchScalarGridSpec(
        num_scalar_prefetch=2,
        grid=(pair_dev // PAIR_BLOCK,),
        in_specs=[
            pl.BlockSpec((PAIR_BLOCK, slot_dev, width, width), lambda i, *_: (i, 0, 0, 0)),
            pl.BlockSpec((ncol, width, width), lambda i, *_: (0, 0, 0)),
        ],
        out_specs=pl.BlockSpec(
            (col_size, PAIR_BLOCK, rows, width), lambda i, *_: (0, i, 0, 0)
        ),
    )
    flops = 4 * pair_dev * slot_dev * width**3
    return pl.pallas_call(
        functools.partial(couple_kernel, slot_dev),
        grid_spec=grid_spec,
        out_shape=jax.ShapeDtypeStruct((col_size, pair_dev, rows, width), jnp.float32),
        compiler_params=pltpu.CompilerParams(vmem_limit_bytes=48 * 1024 * 1024),
        cost_estimate=pl.CostEstimate(
            flops=flops,
            bytes_accessed=tiles.size * 2 + colamp.size * 2 + pair_dev * width * width * 4,
            transcendentals=0,
        ),
    )(links.reshape(-1), nlive, tiles, colamp)


def column_amplitudes(amplitudes, one_hot, pair_size, col_size):
    pair_dev, rows, width = amplitudes.shape
    ncol = one_hot.shape[0]
    contrib = jnp.dot(
        one_hot, amplitudes.reshape(pair_dev, rows * width), precision=lax.Precision.HIGHEST
    )
    per = ncol // pair_size
    parts = lax.all_to_all(contrib, "pair", 0, 0, tiled=True)
    mine = jnp.sum(parts.reshape(pair_size, per, rows * width), axis=0)
    mine = mine.astype(jnp.bfloat16).reshape(1, per, rows, width)
    everyone = pair_size * col_size
    sent = jnp.broadcast_to(mine, (everyone, per, rows, width))
    got = lax.all_to_all(sent, ("pair", "col"), 0, 0, tiled=True)
    got = got.reshape(pair_size, col_size, per, rows, width)
    return got.transpose(0, 2, 1, 3, 4).reshape(ncol, col_size * rows, width)


def per_device(integrals, pno_energy, shift, intersections, links, counts, column_of):
    pair_dev = integrals.shape[0]
    row_count = integrals.shape[1]
    slot_dev = intersections.shape[1]
    col_size = lax.axis_size("col")
    pair_size = lax.axis_size("pair")
    ncol_all = COL_DEV * col_size
    rank = lax.axis_index("col")
    row_energy = lax.dynamic_slice_in_dim(pno_energy, rank * row_count, row_count, 1)
    denom = row_energy[:, :, None] + pno_energy[:, None, :] + shift[:, None, None]
    kfloat = integrals.astype(jnp.float32)
    amplitudes = -kfloat / denom
    one_hot = (jnp.arange(ncol_all, dtype=jnp.int32)[:, None] == column_of[None, :]).astype(
        jnp.float32
    )
    nlive = jnp.clip(counts - rank * slot_dev, 0, slot_dev).astype(jnp.int32)
    for sweep in range(SWEEPS):
        colamp = column_amplitudes(amplitudes, one_hot, pair_size, col_size)
        partial = couple(intersections, colamp, links, nlive, col_size)
        parts = lax.all_to_all(partial, "col", 0, 0, tiled=True)
        coupled = jnp.sum(parts, axis=0)
        amplitudes = -(kfloat + coupled) / denom
    pair_energy = lax.psum(jnp.sum(kfloat * amplitudes, axis=(1, 2)), "col")
    return (amplitudes, pair_energy)


def solution(mesh):
    placed = (
        P("pair", "col", None),
        P("pair", None),
        P("pair"),
        P("pair", "col", None, None),
        P("pair", "col"),
        P("pair"),
        P("pair"),
    )
    return jax.shard_map(
        per_device,
        mesh=mesh,
        in_specs=placed,
        out_specs=(P("pair", "col", None), P("pair")),
        check_vma=False,
    )
```

```python
import functools

import jax
import jax.numpy as jnp
from jax import lax
from jax.experimental import pallas as pl
from jax.experimental.pallas import tpu as pltpu
from jax.sharding import PartitionSpec as P

COL_DEV = 8
SWEEPS = 3
PAIR_BLOCK = 8


def couple_kernel(slot_dev, links_ref, nlive_ref, tiles_ref, colamp_ref, out_ref):
    step = pl.program_id(0)
    width = tiles_ref.shape[-1]
    for q in range(PAIR_BLOCK):
        pair = step * PAIR_BLOCK + q
        live = nlive_ref[pair]
        lefts = []
        for m in range(slot_dev):
            block = colamp_ref[links_ref[pair * slot_dev + m]]
            left = jnp.dot(tiles_ref[q, m], block, preferred_element_type=jnp.float32)
            lefts.append(jnp.where(m < live, left, 0.0).astype(jnp.bfloat16))
        lcat = jnp.concatenate(lefts, axis=1)
        tcat = jnp.concatenate([tiles_ref[q, m] for m in range(slot_dev)], axis=1)
        acc = lax.dot_general(
            lcat, tcat, (((1,), (1,)), ((), ())), preferred_element_type=jnp.float32
        )
        out_ref[:, q] = acc.reshape(out_ref.shape[0], out_ref.shape[2], width)


def couple(tiles, colamp, links, nlive, col_size):
    pair_dev, slot_dev, width, _ = tiles.shape
    ncol = colamp.shape[0]
    rows = width // col_size
    grid_spec = pltpu.PrefetchScalarGridSpec(
        num_scalar_prefetch=2,
        grid=(pair_dev // PAIR_BLOCK,),
        in_specs=[
            pl.BlockSpec((PAIR_BLOCK, slot_dev, width, width), lambda i, *_: (i, 0, 0, 0)),
            pl.BlockSpec((ncol, width, width), lambda i, *_: (0, 0, 0)),
        ],
        out_specs=pl.BlockSpec(
            (col_size, PAIR_BLOCK, rows, width), lambda i, *_: (0, i, 0, 0)
        ),
    )
    flops = 4 * pair_dev * slot_dev * width**3
    return pl.pallas_call(
        functools.partial(couple_kernel, slot_dev),
        grid_spec=grid_spec,
        out_shape=jax.ShapeDtypeStruct((col_size, pair_dev, rows, width), jnp.float32),
        compiler_params=pltpu.CompilerParams(vmem_limit_bytes=48 * 1024 * 1024),
        cost_estimate=pl.CostEstimate(
            flops=flops,
            bytes_accessed=tiles.size * 2 + colamp.size * 2 + pair_dev * width * width * 4,
            transcendentals=0,
        ),
    )(links.reshape(-1), nlive, tiles, colamp)


def column_amplitudes(amplitudes, one_hot, pair_size, col_size):
    pair_dev, rows, width = amplitudes.shape
    ncol = one_hot.shape[0]
    contrib = jnp.dot(
        one_hot, amplitudes.reshape(pair_dev, rows * width), precision=lax.Precision.HIGHEST
    )
    per = ncol // pair_size
    parts = lax.all_to_all(contrib, "pair", 0, 0, tiled=True)
    mine = jnp.sum(parts.reshape(pair_size, per, rows * width), axis=0)
    mine = mine.astype(jnp.bfloat16).reshape(1, per, rows, width)
    everyone = pair_size * col_size
    sent = jnp.broadcast_to(mine, (everyone, per, rows, width))
    got = lax.all_to_all(sent, ("pair", "col"), 0, 0, tiled=True)
    got = got.reshape(pair_size, col_size, per, rows, width)
    return got.transpose(0, 2, 1, 3, 4).reshape(ncol, col_size * rows, width)


def per_device(integrals, pno_energy, shift, intersections, links, counts, column_of):
    pair_dev = integrals.shape[0]
    row_count = integrals.shape[1]
    slot_dev = intersections.shape[1]
    col_size = lax.axis_size("col")
    pair_size = lax.axis_size("pair")
    ncol_all = COL_DEV * col_size
    rank = lax.axis_index("col")
    row_energy = lax.dynamic_slice_in_dim(pno_energy, rank * row_count, row_count, 1)
    denom = row_energy[:, :, None] + pno_energy[:, None, :] + shift[:, None, None]
    kfloat = integrals.astype(jnp.float32)
    amplitudes = -kfloat / denom
    one_hot = (jnp.arange(ncol_all, dtype=jnp.int32)[:, None] == column_of[None, :]).astype(
        jnp.float32
    )
    nlive = jnp.clip(counts - rank * slot_dev, 0, slot_dev).astype(jnp.int32)
    for sweep in range(SWEEPS):
        colamp = column_amplitudes(amplitudes, one_hot, pair_size, col_size)
        partial = couple(intersections, colamp, links, nlive, col_size)
        parts = lax.all_to_all(partial, "col", 0, 0, tiled=True)
        coupled = jnp.sum(parts, axis=0)
        amplitudes = -(kfloat + coupled) / denom
    pair_energy = lax.psum(jnp.sum(kfloat * amplitudes, axis=(1, 2)), "col")
    return (amplitudes, pair_energy)


def solution(mesh):
    placed = (
        P("pair", "col", None),
        P("pair", None),
        P("pair"),
        P("pair", "col", None, None),
        P("pair", "col"),
        P("pair"),
        P("pair"),
    )
    return jax.shard_map(
        per_device,
        mesh=mesh,
        in_specs=placed,
        out_specs=(P("pair", "col", None), P("pair")),
        check_vma=False,
    )
```

```python
import functools

import jax
import jax.numpy as jnp
from jax import lax
from jax.experimental import pallas as pl
from jax.experimental.pallas import tpu as pltpu
from jax.sharding import PartitionSpec as P

COL_DEV = 8
SWEEPS = 3
PAIR_BLOCK = 8


def couple_kernel(slot_dev, links_ref, nlive_ref, tiles_ref, colamp_ref, out_ref):
    step = pl.program_id(0)
    width = tiles_ref.shape[-1]
    for q in range(PAIR_BLOCK):
        pair = step * PAIR_BLOCK + q
        live = nlive_ref[pair]
        lefts = []
        for m in range(slot_dev):
            block = colamp_ref[links_ref[pair * slot_dev + m]]
            left = jnp.dot(tiles_ref[q, m], block, preferred_element_type=jnp.float32)
            lefts.append(jnp.where(m < live, left, 0.0).astype(jnp.bfloat16))
        lcat = jnp.concatenate(lefts, axis=1)
        tcat = jnp.concatenate([tiles_ref[q, m] for m in range(slot_dev)], axis=1)
        acc = lax.dot_general(
            lcat, tcat, (((1,), (1,)), ((), ())), preferred_element_type=jnp.float32
        )
        out_ref[:, q] = acc.reshape(out_ref.shape[0], out_ref.shape[2], width).astype(out_ref.dtype)


def couple(tiles, colamp, links, nlive, col_size):
    pair_dev, slot_dev, width, _ = tiles.shape
    ncol = colamp.shape[0]
    rows = width // col_size
    grid_spec = pltpu.PrefetchScalarGridSpec(
        num_scalar_prefetch=2,
        grid=(pair_dev // PAIR_BLOCK,),
        in_specs=[
            pl.BlockSpec((PAIR_BLOCK, slot_dev, width, width), lambda i, *_: (i, 0, 0, 0)),
            pl.BlockSpec((ncol, width, width), lambda i, *_: (0, 0, 0)),
        ],
        out_specs=pl.BlockSpec(
            (col_size, PAIR_BLOCK, rows, width), lambda i, *_: (0, i, 0, 0)
        ),
    )
    flops = 4 * pair_dev * slot_dev * width**3
    return pl.pallas_call(
        functools.partial(couple_kernel, slot_dev),
        grid_spec=grid_spec,
        out_shape=jax.ShapeDtypeStruct((col_size, pair_dev, rows, width), jnp.bfloat16),
        compiler_params=pltpu.CompilerParams(vmem_limit_bytes=48 * 1024 * 1024),
        cost_estimate=pl.CostEstimate(
            flops=flops,
            bytes_accessed=tiles.size * 2 + colamp.size * 2 + pair_dev * width * width * 2,
            transcendentals=0,
        ),
    )(links.reshape(-1), nlive, tiles, colamp)


def column_amplitudes(amplitudes, one_hot, pair_size, col_size):
    pair_dev, rows, width = amplitudes.shape
    ncol = one_hot.shape[0]
    contrib = jnp.dot(
        one_hot, amplitudes.reshape(pair_dev, rows * width), precision=lax.Precision.HIGHEST
    )
    per = ncol // pair_size
    parts = lax.all_to_all(contrib, "pair", 0, 0, tiled=True)
    mine = jnp.sum(parts.reshape(pair_size, per, rows * width), axis=0)
    mine = mine.astype(jnp.bfloat16).reshape(1, per, rows, width)
    everyone = pair_size * col_size
    sent = jnp.broadcast_to(mine, (everyone, per, rows, width))
    got = lax.all_to_all(sent, ("pair", "col"), 0, 0, tiled=True)
    got = got.reshape(pair_size, col_size, per, rows, width)
    return got.transpose(0, 2, 1, 3, 4).reshape(ncol, col_size * rows, width)


def per_device(integrals, pno_energy, shift, intersections, links, counts, column_of):
    pair_dev = integrals.shape[0]
    row_count = integrals.shape[1]
    slot_dev = intersections.shape[1]
    col_size = lax.axis_size("col")
    pair_size = lax.axis_size("pair")
    ncol_all = COL_DEV * col_size
    rank = lax.axis_index("col")
    row_energy = lax.dynamic_slice_in_dim(pno_energy, rank * row_count, row_count, 1)
    denom = row_energy[:, :, None] + pno_energy[:, None, :] + shift[:, None, None]
    kfloat = integrals.astype(jnp.float32)
    amplitudes = -kfloat / denom
    one_hot = (jnp.arange(ncol_all, dtype=jnp.int32)[:, None] == column_of[None, :]).astype(
        jnp.float32
    )
    nlive = jnp.clip(counts - rank * slot_dev, 0, slot_dev).astype(jnp.int32)
    for sweep in range(SWEEPS):
        colamp = column_amplitudes(amplitudes, one_hot, pair_size, col_size)
        partial = couple(intersections, colamp, links, nlive, col_size)
        parts = lax.all_to_all(partial, "col", 0, 0, tiled=True)
        coupled = jnp.sum(parts.astype(jnp.float32), axis=0)
        amplitudes = -(kfloat + coupled) / denom
    pair_energy = lax.psum(jnp.sum(kfloat * amplitudes, axis=(1, 2)), "col")
    return (amplitudes, pair_energy)


def solution(mesh):
    placed = (
        P("pair", "col", None),
        P("pair", None),
        P("pair"),
        P("pair", "col", None, None),
        P("pair", "col"),
        P("pair"),
        P("pair"),
    )
    return jax.shard_map(
        per_device,
        mesh=mesh,
        in_specs=placed,
        out_specs=(P("pair", "col", None), P("pair")),
        check_vma=False,
    )
```

```python
import functools

import jax
import jax.numpy as jnp
from jax import lax
from jax.experimental import pallas as pl
from jax.experimental.pallas import tpu as pltpu
from jax.sharding import PartitionSpec as P

COL_DEV = 8
SWEEPS = 3
PAIR_BLOCK = 8


def couple_kernel(slot_dev, links_ref, nlive_ref, tiles_ref, colamp_ref, out_ref):
    step = pl.program_id(0)
    width = tiles_ref.shape[-1]
    for q in range(PAIR_BLOCK):
        pair = step * PAIR_BLOCK + q
        live = nlive_ref[pair]
        lefts = []
        for m in range(slot_dev):
            block = colamp_ref[links_ref[pair * slot_dev + m]]
            left = jnp.dot(tiles_ref[q, m], block, preferred_element_type=jnp.float32)
            lefts.append(jnp.where(m < live, left, 0.0).astype(jnp.bfloat16))
        lcat = jnp.concatenate(lefts, axis=1)
        tcat = jnp.concatenate([tiles_ref[q, m] for m in range(slot_dev)], axis=1)
        acc = lax.dot_general(
            lcat, tcat, (((1,), (1,)), ((), ())), preferred_element_type=jnp.float32
        )
        out_ref[:, q] = acc.reshape(out_ref.shape[0], out_ref.shape[2], width).astype(out_ref.dtype)


def couple(tiles, colamp, links, nlive, col_size):
    pair_dev, slot_dev, width, _ = tiles.shape
    ncol = colamp.shape[0]
    rows = width // col_size
    grid_spec = pltpu.PrefetchScalarGridSpec(
        num_scalar_prefetch=2,
        grid=(pair_dev // PAIR_BLOCK,),
        in_specs=[
            pl.BlockSpec((PAIR_BLOCK, slot_dev, width, width), lambda i, *_: (i, 0, 0, 0)),
            pl.BlockSpec((ncol, width, width), lambda i, *_: (0, 0, 0)),
        ],
        out_specs=pl.BlockSpec(
            (col_size, PAIR_BLOCK, rows, width), lambda i, *_: (0, i, 0, 0)
        ),
    )
    flops = 4 * pair_dev * slot_dev * width**3
    return pl.pallas_call(
        functools.partial(couple_kernel, slot_dev),
        grid_spec=grid_spec,
        out_shape=jax.ShapeDtypeStruct((col_size, pair_dev, rows, width), jnp.bfloat16),
        compiler_params=pltpu.CompilerParams(vmem_limit_bytes=48 * 1024 * 1024),
        cost_estimate=pl.CostEstimate(
            flops=flops,
            bytes_accessed=tiles.size * 2 + colamp.size * 2 + pair_dev * width * width * 2,
            transcendentals=0,
        ),
    )(links.reshape(-1), nlive, tiles, colamp)


def column_amplitudes(amplitudes, one_hot, pair_size, col_size):
    pair_dev, rows, width = amplitudes.shape
    ncol = one_hot.shape[0]
    contrib = jnp.dot(
        one_hot, amplitudes.reshape(pair_dev, rows * width), precision=lax.Precision.HIGHEST
    )
    per = ncol // pair_size
    parts = lax.all_to_all(contrib, "pair", 0, 0, tiled=True)
    mine = jnp.sum(parts.reshape(pair_size, per, rows * width), axis=0)
    mine = mine.astype(jnp.bfloat16).reshape(1, per, rows, width)
    everyone = pair_size * col_size
    sent = jnp.broadcast_to(mine, (everyone, per, rows, width))
    got = lax.all_to_all(sent, ("pair", "col"), 0, 0, tiled=True)
    got = got.reshape(pair_size, col_size, per, rows, width)
    return got.transpose(0, 2, 1, 3, 4).reshape(ncol, col_size * rows, width)


def per_device(integrals, pno_energy, shift, intersections, links, counts, column_of):
    pair_dev = integrals.shape[0]
    row_count = integrals.shape[1]
    slot_dev = intersections.shape[1]
    col_size = lax.axis_size("col")
    pair_size = lax.axis_size("pair")
    ncol_all = COL_DEV * col_size
    rank = lax.axis_index("col")
    row_energy = lax.dynamic_slice_in_dim(pno_energy, rank * row_count, row_count, 1)
    denom = row_energy[:, :, None] + pno_energy[:, None, :] + shift[:, None, None]
    kfloat = integrals.astype(jnp.float32)
    amplitudes = -kfloat / denom
    one_hot = (jnp.arange(ncol_all, dtype=jnp.int32)[:, None] == column_of[None, :]).astype(
        jnp.float32
    )
    nlive = jnp.clip(counts - rank * slot_dev, 0, slot_dev).astype(jnp.int32)
    blocks = [integrals]
    for k in range(1, col_size):
        ring = [(i, (i + k) % col_size) for i in range(col_size)]
        blocks.append(lax.ppermute(integrals, "col", ring))
    owner_of = (rank - jnp.arange(col_size)) % col_size
    k_full = jnp.take(jnp.stack(blocks), owner_of, axis=0).astype(jnp.float32)
    full_energy = pno_energy.reshape(pair_dev, col_size, 1, row_count, 1)
    denom_full = full_energy + pno_energy[:, None, None, None, :] + shift[:, None, None, None, None]
    weight = k_full / jnp.swapaxes(denom_full[:, :, 0], 0, 1)
    for sweep in range(SWEEPS):
        colamp = column_amplitudes(amplitudes, one_hot, pair_size, col_size)
        partial = couple(intersections, colamp, links, nlive, col_size)
        if sweep < SWEEPS - 1:
            parts = lax.all_to_all(partial, "col", 0, 0, tiled=True)
            coupled = jnp.sum(parts.astype(jnp.float32), axis=0)
        else:
            share = -jnp.sum(weight * partial.astype(jnp.float32), axis=(0, 2, 3))
            high = share.astype(jnp.bfloat16)
            low = (share - high.astype(jnp.float32)).astype(jnp.bfloat16)
            extra = jnp.zeros((row_count, partial.shape[-1]), jnp.bfloat16)
            extra = extra.at[0, :pair_dev].set(high).at[1, :pair_dev].set(low)
            extra = jnp.broadcast_to(extra, (col_size, 1) + extra.shape)
            parts = lax.all_to_all(jnp.concatenate([partial, extra], axis=1), "col", 0, 0, tiled=True)
            parts = parts.astype(jnp.float32)
            coupled = jnp.sum(parts[:, :pair_dev], axis=0)
            shares = parts[:, pair_dev, 0, :pair_dev] + parts[:, pair_dev, 1, :pair_dev]
        amplitudes = -(kfloat + coupled) / denom
    base = -jnp.sum(weight * k_full, axis=(0, 2, 3))
    pair_energy = base + jnp.sum(shares, axis=0)
    return (amplitudes, pair_energy)


def solution(mesh):
    placed = (
        P("pair", "col", None),
        P("pair", None),
        P("pair"),
        P("pair", "col", None, None),
        P("pair", "col"),
        P("pair"),
        P("pair"),
    )
    return jax.shard_map(
        per_device,
        mesh=mesh,
        in_specs=placed,
        out_specs=(P("pair", "col", None), P("pair")),
        check_vma=False,
    )
```

```python
import functools

import jax
import jax.numpy as jnp
from jax import lax
from jax.experimental import pallas as pl
from jax.experimental.pallas import tpu as pltpu
from jax.sharding import PartitionSpec as P

COL_DEV = 8
SWEEPS = 3
PAIR_BLOCK = 8


def couple_kernel(slot_dev, links_ref, nlive_ref, tiles_ref, colamp_ref, out_ref):
    step = pl.program_id(0)
    width = tiles_ref.shape[-1]
    for q in range(PAIR_BLOCK):
        pair = step * PAIR_BLOCK + q
        live = nlive_ref[pair]
        lefts = []
        for m in range(slot_dev):
            block = colamp_ref[links_ref[pair * slot_dev + m]]
            left = jnp.dot(tiles_ref[q, m], block, preferred_element_type=jnp.float32)
            lefts.append(jnp.where(m < live, left, 0.0).astype(jnp.bfloat16))
        lcat = jnp.concatenate(lefts, axis=1)
        tcat = jnp.concatenate([tiles_ref[q, m] for m in range(slot_dev)], axis=1)
        acc = lax.dot_general(
            lcat, tcat, (((1,), (1,)), ((), ())), preferred_element_type=jnp.float32
        )
        out_ref[:, q] = acc.reshape(out_ref.shape[0], out_ref.shape[2], width).astype(out_ref.dtype)


def couple(tiles, colamp, links, nlive, col_size):
    pair_dev, slot_dev, width, _ = tiles.shape
    ncol = colamp.shape[0]
    rows = width // col_size
    grid_spec = pltpu.PrefetchScalarGridSpec(
        num_scalar_prefetch=2,
        grid=(pair_dev // PAIR_BLOCK,),
        in_specs=[
            pl.BlockSpec((PAIR_BLOCK, slot_dev, width, width), lambda i, *_: (i, 0, 0, 0)),
            pl.BlockSpec((ncol, width, width), lambda i, *_: (0, 0, 0)),
        ],
        out_specs=pl.BlockSpec(
            (col_size, PAIR_BLOCK, rows, width), lambda i, *_: (0, i, 0, 0)
        ),
    )
    flops = 4 * pair_dev * slot_dev * width**3
    return pl.pallas_call(
        functools.partial(couple_kernel, slot_dev),
        grid_spec=grid_spec,
        out_shape=jax.ShapeDtypeStruct((col_size, pair_dev, rows, width), jnp.bfloat16),
        compiler_params=pltpu.CompilerParams(vmem_limit_bytes=48 * 1024 * 1024),
        cost_estimate=pl.CostEstimate(
            flops=flops,
            bytes_accessed=tiles.size * 2 + colamp.size * 2 + pair_dev * width * width * 2,
            transcendentals=0,
        ),
    )(links.reshape(-1), nlive, tiles, colamp)


def column_amplitudes(amplitudes, one_hot, pair_size, col_size):
    pair_dev, rows, width = amplitudes.shape
    ncol = one_hot.shape[0]
    contrib = jnp.dot(
        one_hot, amplitudes.reshape(pair_dev, rows * width), precision=lax.Precision.HIGHEST
    )
    per = ncol // pair_size
    parts = lax.all_to_all(contrib, "pair", 0, 0, tiled=True)
    mine = jnp.sum(parts.reshape(pair_size, per, rows * width), axis=0)
    mine = mine.astype(jnp.bfloat16).reshape(1, per, rows, width)
    everyone = pair_size * col_size
    sent = jnp.broadcast_to(mine, (everyone, per, rows, width))
    got = lax.all_to_all(sent, ("pair", "col"), 0, 0, tiled=True)
    got = got.reshape(pair_size, col_size, per, rows, width)
    return got.transpose(0, 2, 1, 3, 4).reshape(ncol, col_size * rows, width)


def per_device(integrals, pno_energy, shift, intersections, links, counts, column_of):
    pair_dev = integrals.shape[0]
    row_count = integrals.shape[1]
    slot_dev = intersections.shape[1]
    col_size = lax.axis_size("col")
    pair_size = lax.axis_size("pair")
    ncol_all = COL_DEV * col_size
    rank = lax.axis_index("col")
    row_energy = lax.dynamic_slice_in_dim(pno_energy, rank * row_count, row_count, 1)
    denom = row_energy[:, :, None] + pno_energy[:, None, :] + shift[:, None, None]
    kfloat = integrals.astype(jnp.float32)
    amplitudes = -kfloat / denom
    one_hot = (jnp.arange(ncol_all, dtype=jnp.int32)[:, None] == column_of[None, :]).astype(
        jnp.float32
    )
    nlive = jnp.clip(counts - rank * slot_dev, 0, slot_dev).astype(jnp.int32)
    blocks = [integrals]
    for k in range(1, col_size):
        ring = [(i, (i + k) % col_size) for i in range(col_size)]
        blocks.append(lax.ppermute(integrals, "col", ring))
    owner_of = (rank - jnp.arange(col_size)) % col_size
    full_energy = pno_energy.reshape(pair_dev, col_size, 1, row_count, 1)
    denom_full = full_energy + pno_energy[:, None, None, None, :] + shift[:, None, None, None, None]
    for sweep in range(SWEEPS):
        colamp = column_amplitudes(amplitudes, one_hot, pair_size, col_size)
        partial = couple(intersections, colamp, links, nlive, col_size)
        if sweep == 0:
            partial, blocks = lax.optimization_barrier((partial, blocks))
            k_full = jnp.take(jnp.stack(blocks), owner_of, axis=0).astype(jnp.float32)
            weight = k_full / jnp.swapaxes(denom_full[:, :, 0], 0, 1)
        if sweep < SWEEPS - 1:
            parts = lax.all_to_all(partial, "col", 0, 0, tiled=True)
            coupled = jnp.sum(parts.astype(jnp.float32), axis=0)
        else:
            share = -jnp.sum(weight * partial.astype(jnp.float32), axis=(0, 2, 3))
            high = share.astype(jnp.bfloat16)
            low = (share - high.astype(jnp.float32)).astype(jnp.bfloat16)
            extra = jnp.zeros((row_count, partial.shape[-1]), jnp.bfloat16)
            extra = extra.at[0, :pair_dev].set(high).at[1, :pair_dev].set(low)
            extra = jnp.broadcast_to(extra, (col_size, 1) + extra.shape)
            parts = lax.all_to_all(jnp.concatenate([partial, extra], axis=1), "col", 0, 0, tiled=True)
            parts = parts.astype(jnp.float32)
            coupled = jnp.sum(parts[:, :pair_dev], axis=0)
            shares = parts[:, pair_dev, 0, :pair_dev] + parts[:, pair_dev, 1, :pair_dev]
        amplitudes = -(kfloat + coupled) / denom
    base = -jnp.sum(weight * k_full, axis=(0, 2, 3))
    pair_energy = base + jnp.sum(shares, axis=0)
    return (amplitudes, pair_energy)


def solution(mesh):
    placed = (
        P("pair", "col", None),
        P("pair", None),
        P("pair"),
        P("pair", "col", None, None),
        P("pair", "col"),
        P("pair"),
        P("pair"),
    )
    return jax.shard_map(
        per_device,
        mesh=mesh,
        in_specs=placed,
        out_specs=(P("pair", "col", None), P("pair")),
        check_vma=False,
    )
```

```python
import functools

import jax
import jax.numpy as jnp
from jax import lax
from jax.experimental import pallas as pl
from jax.experimental.pallas import tpu as pltpu
from jax.sharding import PartitionSpec as P

COL_DEV = 8
SWEEPS = 3
PAIR_BLOCK = 8


def couple_kernel(slot_dev, links_ref, nlive_ref, tiles_ref, colamp_ref, out_ref):
    step = pl.program_id(0)
    width = tiles_ref.shape[-1]
    for q in range(PAIR_BLOCK):
        pair = step * PAIR_BLOCK + q
        live = nlive_ref[pair]
        lefts = []
        for m in range(slot_dev):
            block = colamp_ref[links_ref[pair * slot_dev + m]]
            left = jnp.dot(tiles_ref[q, m], block, preferred_element_type=jnp.float32)
            lefts.append(jnp.where(m < live, left, 0.0).astype(jnp.bfloat16))
        lcat = jnp.concatenate(lefts, axis=1)
        tcat = jnp.concatenate([tiles_ref[q, m] for m in range(slot_dev)], axis=1)
        acc = lax.dot_general(
            lcat, tcat, (((1,), (1,)), ((), ())), preferred_element_type=jnp.float32
        )
        out_ref[:, q] = acc.reshape(out_ref.shape[0], out_ref.shape[2], width).astype(out_ref.dtype)


def couple(tiles, colamp, links, nlive, col_size):
    pair_dev, slot_dev, width, _ = tiles.shape
    ncol = colamp.shape[0]
    rows = width // col_size
    grid_spec = pltpu.PrefetchScalarGridSpec(
        num_scalar_prefetch=2,
        grid=(pair_dev // PAIR_BLOCK,),
        in_specs=[
            pl.BlockSpec((PAIR_BLOCK, slot_dev, width, width), lambda i, *_: (i, 0, 0, 0)),
            pl.BlockSpec((ncol, width, width), lambda i, *_: (0, 0, 0)),
        ],
        out_specs=pl.BlockSpec(
            (col_size, PAIR_BLOCK, rows, width), lambda i, *_: (0, i, 0, 0)
        ),
    )
    flops = 4 * pair_dev * slot_dev * width**3
    return pl.pallas_call(
        functools.partial(couple_kernel, slot_dev),
        grid_spec=grid_spec,
        out_shape=jax.ShapeDtypeStruct((col_size, pair_dev, rows, width), jnp.bfloat16),
        compiler_params=pltpu.CompilerParams(vmem_limit_bytes=48 * 1024 * 1024),
        cost_estimate=pl.CostEstimate(
            flops=flops,
            bytes_accessed=tiles.size * 2 + colamp.size * 2 + pair_dev * width * width * 2,
            transcendentals=0,
        ),
    )(links.reshape(-1), nlive, tiles, colamp)


def column_amplitudes(amplitudes, one_hot, pair_size, col_size):
    pair_dev, rows, width = amplitudes.shape
    ncol = one_hot.shape[0]
    contrib = jnp.dot(
        one_hot, amplitudes.reshape(pair_dev, rows * width), precision=lax.Precision.HIGHEST
    )
    per = ncol // pair_size
    parts = lax.all_to_all(contrib, ("core", "ph"), 0, 0, tiled=True)
    mine = jnp.sum(parts.reshape(pair_size, per, rows * width), axis=0)
    mine = mine.astype(jnp.bfloat16).reshape(1, per, rows, width)
    peers = pair_size // 2 * col_size
    sent = jnp.broadcast_to(mine, (peers, per, rows, width))
    got = lax.all_to_all(sent, ("ph", "col"), 0, 0, tiled=True)
    other = lax.ppermute(got, "core", [(0, 1), (1, 0)])
    both = jnp.stack([got, other]).reshape(2, pair_size // 2, col_size, per, rows, width)
    return both.transpose(0, 1, 3, 2, 4, 5).reshape(ncol, col_size * rows, width)


def per_device(integrals, pno_energy, shift, intersections, links, counts, column_of):
    pair_dev = integrals.shape[0]
    row_count = integrals.shape[1]
    slot_dev = intersections.shape[1]
    col_size = lax.axis_size("col")
    pair_size = lax.axis_size("ph") * lax.axis_size("core")
    ncol_all = COL_DEV * col_size
    rank = lax.axis_index("col")
    row_energy = lax.dynamic_slice_in_dim(pno_energy, rank * row_count, row_count, 1)
    denom = row_energy[:, :, None] + pno_energy[:, None, :] + shift[:, None, None]
    kfloat = integrals.astype(jnp.float32)
    amplitudes = -kfloat / denom
    one_hot = (jnp.arange(ncol_all, dtype=jnp.int32)[:, None] == column_of[None, :]).astype(
        jnp.float32
    )
    nlive = jnp.clip(counts - rank * slot_dev, 0, slot_dev).astype(jnp.int32)
    local_links = (links + ncol_all // 2 * lax.axis_index("core")) % ncol_all
    blocks = [integrals]
    for k in range(1, col_size):
        ring = [(i, (i + k) % col_size) for i in range(col_size)]
        blocks.append(lax.ppermute(integrals, "col", ring))
    owner_of = (rank - jnp.arange(col_size)) % col_size
    full_energy = pno_energy.reshape(pair_dev, col_size, 1, row_count, 1)
    denom_full = full_energy + pno_energy[:, None, None, None, :] + shift[:, None, None, None, None]
    for sweep in range(SWEEPS):
        colamp = column_amplitudes(amplitudes, one_hot, pair_size, col_size)
        partial = couple(intersections, colamp, local_links, nlive, col_size)
        if sweep == 0:
            partial, blocks = lax.optimization_barrier((partial, blocks))
            k_full = jnp.take(jnp.stack(blocks), owner_of, axis=0).astype(jnp.float32)
            weight = k_full / jnp.swapaxes(denom_full[:, :, 0], 0, 1)
        if sweep < SWEEPS - 1:
            parts = lax.all_to_all(partial, "col", 0, 0, tiled=True)
            coupled = jnp.sum(parts.astype(jnp.float32), axis=0)
        else:
            share = -jnp.sum(weight * partial.astype(jnp.float32), axis=(0, 2, 3))
            high = share.astype(jnp.bfloat16)
            low = (share - high.astype(jnp.float32)).astype(jnp.bfloat16)
            extra = jnp.zeros((row_count, partial.shape[-1]), jnp.bfloat16)
            extra = extra.at[0, :pair_dev].set(high).at[1, :pair_dev].set(low)
            extra = jnp.broadcast_to(extra, (col_size, 1) + extra.shape)
            parts = lax.all_to_all(jnp.concatenate([partial, extra], axis=1), "col", 0, 0, tiled=True)
            parts = parts.astype(jnp.float32)
            coupled = jnp.sum(parts[:, :pair_dev], axis=0)
            shares = parts[:, pair_dev, 0, :pair_dev] + parts[:, pair_dev, 1, :pair_dev]
        amplitudes = -(kfloat + coupled) / denom
    base = -jnp.sum(weight * k_full, axis=(0, 2, 3))
    pair_energy = base + jnp.sum(shares, axis=0)
    return (amplitudes, pair_energy)


def solution(mesh):
    col_size, pair_size = mesh.devices.shape
    split = jax.sharding.Mesh(
        mesh.devices.reshape(col_size, pair_size // 2, 2), ("col", "ph", "core")
    )
    pair = ("ph", "core")
    placed = (
        P(pair, "col", None),
        P(pair, None),
        P(pair),
        P(pair, "col", None, None),
        P(pair, "col"),
        P(pair),
        P(pair),
    )
    return jax.shard_map(
        per_device,
        mesh=split,
        in_specs=placed,
        out_specs=(P(pair, "col", None), P(pair)),
        check_vma=False,
    )
```

```python
import functools

import jax
import jax.numpy as jnp
from jax import lax
from jax.experimental import pallas as pl
from jax.experimental.pallas import tpu as pltpu
from jax.sharding import PartitionSpec as P

COL_DEV = 8
SWEEPS = 3
PAIR_BLOCK = 8


def couple_kernel(slot_dev, links_ref, nlive_ref, tiles_ref, colamp_ref, out_ref):
    step = pl.program_id(0)
    width = tiles_ref.shape[-1]
    for q in range(PAIR_BLOCK):
        pair = step * PAIR_BLOCK + q
        live = nlive_ref[pair]
        lefts = []
        for m in range(slot_dev):
            block = colamp_ref[links_ref[pair * slot_dev + m]]
            left = jnp.dot(tiles_ref[q, m], block, preferred_element_type=jnp.float32)
            lefts.append(jnp.where(m < live, left, 0.0).astype(jnp.bfloat16))
        lcat = jnp.concatenate(lefts, axis=1)
        tcat = jnp.concatenate([tiles_ref[q, m] for m in range(slot_dev)], axis=1)
        acc = lax.dot_general(
            lcat, tcat, (((1,), (1,)), ((), ())), preferred_element_type=jnp.float32
        )
        out_ref[:, q] = acc.reshape(out_ref.shape[0], out_ref.shape[2], width).astype(out_ref.dtype)


def couple(tiles, colamp, links, nlive, col_size):
    pair_dev, slot_dev, width, _ = tiles.shape
    ncol = colamp.shape[0]
    rows = width // col_size
    grid_spec = pltpu.PrefetchScalarGridSpec(
        num_scalar_prefetch=2,
        grid=(pair_dev // PAIR_BLOCK,),
        in_specs=[
            pl.BlockSpec((PAIR_BLOCK, slot_dev, width, width), lambda i, *_: (i, 0, 0, 0)),
            pl.BlockSpec((ncol, width, width), lambda i, *_: (0, 0, 0)),
        ],
        out_specs=pl.BlockSpec(
            (col_size, PAIR_BLOCK, rows, width), lambda i, *_: (0, i, 0, 0)
        ),
    )
    flops = 4 * pair_dev * slot_dev * width**3
    return pl.pallas_call(
        functools.partial(couple_kernel, slot_dev),
        grid_spec=grid_spec,
        out_shape=jax.ShapeDtypeStruct((col_size, pair_dev, rows, width), jnp.bfloat16),
        compiler_params=pltpu.CompilerParams(vmem_limit_bytes=48 * 1024 * 1024),
        cost_estimate=pl.CostEstimate(
            flops=flops,
            bytes_accessed=tiles.size * 2 + colamp.size * 2 + pair_dev * width * width * 2,
            transcendentals=0,
        ),
    )(links.reshape(-1), nlive, tiles, colamp)


def column_amplitudes(amplitudes, one_hot, pair_size, col_size):
    pair_dev, rows, width = amplitudes.shape
    ncol = one_hot.shape[0]
    contrib = jnp.dot(
        one_hot, amplitudes.reshape(pair_dev, rows * width), precision=lax.Precision.HIGHEST
    )
    per = ncol // pair_size
    parts = lax.all_to_all(contrib, ("core", "ph"), 0, 0, tiled=True)
    mine = jnp.sum(parts.reshape(pair_size, per, rows * width), axis=0)
    mine = mine.astype(jnp.bfloat16).reshape(1, per, rows, width)
    peers = pair_size // 2 * col_size
    sent = jnp.broadcast_to(mine, (peers, per, rows, width))
    got = lax.all_to_all(sent, ("ph", "col"), 0, 0, tiled=True)
    other = lax.ppermute(got, "core", [(0, 1), (1, 0)])
    both = jnp.stack([got, other]).reshape(2, pair_size // 2, col_size, per, rows, width)
    return both.transpose(0, 1, 3, 2, 4, 5).reshape(ncol, col_size * rows, width)


def per_device(integrals, pno_energy, shift, intersections, links, counts, column_of):
    pair_dev = integrals.shape[0]
    row_count = integrals.shape[1]
    slot_dev = intersections.shape[1]
    col_size = lax.axis_size("col")
    pair_size = lax.axis_size("ph") * lax.axis_size("core")
    ncol_all = COL_DEV * col_size
    rank = lax.axis_index("col")
    row_energy = lax.dynamic_slice_in_dim(pno_energy, rank * row_count, row_count, 1)
    denom = row_energy[:, :, None] + pno_energy[:, None, :] + shift[:, None, None]
    kfloat = integrals.astype(jnp.float32)
    amplitudes = -kfloat / denom
    one_hot = (jnp.arange(ncol_all, dtype=jnp.int32)[:, None] == column_of[None, :]).astype(
        jnp.float32
    )
    nlive = jnp.clip(counts - rank * slot_dev, 0, slot_dev).astype(jnp.int32)
    local_links = (links + ncol_all // 2 * lax.axis_index("core")) % ncol_all
    blocks = lax.all_gather(integrals, "col")
    full_energy = pno_energy.reshape(pair_dev, col_size, 1, row_count, 1)
    denom_full = full_energy + pno_energy[:, None, None, None, :] + shift[:, None, None, None, None]
    for sweep in range(SWEEPS):
        colamp = column_amplitudes(amplitudes, one_hot, pair_size, col_size)
        partial = couple(intersections, colamp, local_links, nlive, col_size)
        if sweep == 0:
            partial, blocks = lax.optimization_barrier((partial, blocks))
            k_full = blocks.astype(jnp.float32)
            weight = k_full / jnp.swapaxes(denom_full[:, :, 0], 0, 1)
        if sweep < SWEEPS - 1:
            parts = lax.all_to_all(partial, "col", 0, 0, tiled=True)
            coupled = jnp.sum(parts.astype(jnp.float32), axis=0)
        else:
            share = -jnp.sum(weight * partial.astype(jnp.float32), axis=(0, 2, 3))
            high = share.astype(jnp.bfloat16)
            low = (share - high.astype(jnp.float32)).astype(jnp.bfloat16)
            extra = jnp.zeros((row_count, partial.shape[-1]), jnp.bfloat16)
            extra = extra.at[0, :pair_dev].set(high).at[1, :pair_dev].set(low)
            extra = jnp.broadcast_to(extra, (col_size, 1) + extra.shape)
            parts = lax.all_to_all(jnp.concatenate([partial, extra], axis=1), "col", 0, 0, tiled=True)
            parts = parts.astype(jnp.float32)
            coupled = jnp.sum(parts[:, :pair_dev], axis=0)
            shares = parts[:, pair_dev, 0, :pair_dev] + parts[:, pair_dev, 1, :pair_dev]
        amplitudes = -(kfloat + coupled) / denom
    base = -jnp.sum(weight * k_full, axis=(0, 2, 3))
    pair_energy = base + jnp.sum(shares, axis=0)
    return (amplitudes, pair_energy)


def solution(mesh):
    col_size, pair_size = mesh.devices.shape
    split = jax.sharding.Mesh(
        mesh.devices.reshape(col_size, pair_size // 2, 2), ("col", "ph", "core")
    )
    pair = ("ph", "core")
    placed = (
        P(pair, "col", None),
        P(pair, None),
        P(pair),
        P(pair, "col", None, None),
        P(pair, "col"),
        P(pair),
        P(pair),
    )
    return jax.shard_map(
        per_device,
        mesh=split,
        in_specs=placed,
        out_specs=(P(pair, "col", None), P(pair)),
        check_vma=False,
    )
```

```python
import functools

import jax
import jax.numpy as jnp
from jax import lax
from jax.experimental import pallas as pl
from jax.experimental.pallas import tpu as pltpu
from jax.sharding import PartitionSpec as P

COL_DEV = 8
SWEEPS = 3
PAIR_BLOCK = 8


def couple_kernel(slot_dev, links_ref, nlive_ref, tiles_ref, colamp_ref, out_ref):
    step = pl.program_id(0)
    width = tiles_ref.shape[-1]
    for q in range(PAIR_BLOCK):
        pair = step * PAIR_BLOCK + q
        live = nlive_ref[pair]
        lefts = []
        for m in range(slot_dev):
            block = colamp_ref[links_ref[pair * slot_dev + m]]
            left = jnp.dot(tiles_ref[q, m], block, preferred_element_type=jnp.float32)
            lefts.append(jnp.where(m < live, left, 0.0).astype(jnp.bfloat16))
        lcat = jnp.concatenate(lefts, axis=1)
        tcat = jnp.concatenate([tiles_ref[q, m] for m in range(slot_dev)], axis=1)
        acc = lax.dot_general(
            lcat, tcat, (((1,), (1,)), ((), ())), preferred_element_type=jnp.float32
        )
        out_ref[:, q] = acc.reshape(out_ref.shape[0], out_ref.shape[2], width).astype(out_ref.dtype)


def couple(tiles, colamp, links, nlive, col_size):
    pair_dev, slot_dev, width, _ = tiles.shape
    ncol = colamp.shape[0]
    rows = width // col_size
    grid_spec = pltpu.PrefetchScalarGridSpec(
        num_scalar_prefetch=2,
        grid=(pair_dev // PAIR_BLOCK,),
        in_specs=[
            pl.BlockSpec((PAIR_BLOCK, slot_dev, width, width), lambda i, *_: (i, 0, 0, 0)),
            pl.BlockSpec((ncol, width, width), lambda i, *_: (0, 0, 0)),
        ],
        out_specs=pl.BlockSpec(
            (col_size, PAIR_BLOCK, rows, width), lambda i, *_: (0, i, 0, 0)
        ),
    )
    flops = 4 * pair_dev * slot_dev * width**3
    return pl.pallas_call(
        functools.partial(couple_kernel, slot_dev),
        grid_spec=grid_spec,
        out_shape=jax.ShapeDtypeStruct((col_size, pair_dev, rows, width), jnp.bfloat16),
        compiler_params=pltpu.CompilerParams(vmem_limit_bytes=48 * 1024 * 1024),
        cost_estimate=pl.CostEstimate(
            flops=flops,
            bytes_accessed=tiles.size * 2 + colamp.size * 2 + pair_dev * width * width * 2,
            transcendentals=0,
        ),
    )(links.reshape(-1), nlive, tiles, colamp)


def column_amplitudes(amplitudes, one_hot, pair_size, col_size):
    pair_dev, rows, width = amplitudes.shape
    ncol = one_hot.shape[0]
    contrib = jnp.dot(
        one_hot, amplitudes.reshape(pair_dev, rows * width), precision=lax.Precision.HIGHEST
    )
    per = ncol // pair_size
    parts = lax.all_to_all(contrib, ("core", "ph"), 0, 0, tiled=True)
    mine = jnp.sum(parts.reshape(pair_size, per, rows * width), axis=0)
    mine = mine.astype(jnp.bfloat16).reshape(1, per, rows, width)
    peers = pair_size // 2 * col_size
    sent = jnp.broadcast_to(mine, (peers, per, rows, width))
    got = lax.all_to_all(sent, ("ph", "col"), 0, 0, tiled=True)
    other = lax.ppermute(got, "core", [(0, 1), (1, 0)])
    both = jnp.stack([got, other]).reshape(2, pair_size // 2, col_size, per, rows, width)
    return both.transpose(0, 1, 3, 2, 4, 5).reshape(ncol, col_size * rows, width)


def per_device(integrals, pno_energy, shift, intersections, links, counts, column_of):
    pair_dev = integrals.shape[0]
    row_count = integrals.shape[1]
    slot_dev = intersections.shape[1]
    col_size = lax.axis_size("col")
    pair_size = lax.axis_size("ph") * lax.axis_size("core")
    ncol_all = COL_DEV * col_size
    rank = lax.axis_index("col")
    row_energy = lax.dynamic_slice_in_dim(pno_energy, rank * row_count, row_count, 1)
    denom = row_energy[:, :, None] + pno_energy[:, None, :] + shift[:, None, None]
    kfloat = integrals.astype(jnp.float32)
    amplitudes = -kfloat / denom
    one_hot = (jnp.arange(ncol_all, dtype=jnp.int32)[:, None] == column_of[None, :]).astype(
        jnp.float32
    )
    nlive = jnp.clip(counts - rank * slot_dev, 0, slot_dev).astype(jnp.int32)
    local_links = (links + ncol_all // 2 * lax.axis_index("core")) % ncol_all
    full_energy = pno_energy.reshape(pair_dev, col_size, 1, row_count, 1)
    denom_full = full_energy + pno_energy[:, None, None, None, :] + shift[:, None, None, None, None]
    for sweep in range(SWEEPS):
        colamp = column_amplitudes(amplitudes, one_hot, pair_size, col_size)
        partial = couple(intersections, colamp, local_links, nlive, col_size)
        if sweep == 0:
            sent = jnp.concatenate([partial, jnp.broadcast_to(integrals, partial.shape)], axis=1)
            parts = lax.all_to_all(sent, "col", 0, 0, tiled=True)
            coupled = jnp.sum(parts[:, :pair_dev].astype(jnp.float32), axis=0)
            k_full = parts[:, pair_dev:].astype(jnp.float32)
            weight = k_full / jnp.swapaxes(denom_full[:, :, 0], 0, 1)
        elif sweep < SWEEPS - 1:
            parts = lax.all_to_all(partial, "col", 0, 0, tiled=True)
            coupled = jnp.sum(parts.astype(jnp.float32), axis=0)
        else:
            share = -jnp.sum(weight * partial.astype(jnp.float32), axis=(0, 2, 3))
            high = share.astype(jnp.bfloat16)
            low = (share - high.astype(jnp.float32)).astype(jnp.bfloat16)
            extra = jnp.zeros((row_count, partial.shape[-1]), jnp.bfloat16)
            extra = extra.at[0, :pair_dev].set(high).at[1, :pair_dev].set(low)
            extra = jnp.broadcast_to(extra, (col_size, 1) + extra.shape)
            parts = lax.all_to_all(jnp.concatenate([partial, extra], axis=1), "col", 0, 0, tiled=True)
            parts = parts.astype(jnp.float32)
            coupled = jnp.sum(parts[:, :pair_dev], axis=0)
            shares = parts[:, pair_dev, 0, :pair_dev] + parts[:, pair_dev, 1, :pair_dev]
        amplitudes = -(kfloat + coupled) / denom
    base = -jnp.sum(weight * k_full, axis=(0, 2, 3))
    pair_energy = base + jnp.sum(shares, axis=0)
    return (amplitudes, pair_energy)


def solution(mesh):
    col_size, pair_size = mesh.devices.shape
    split = jax.sharding.Mesh(
        mesh.devices.reshape(col_size, pair_size // 2, 2), ("col", "ph", "core")
    )
    pair = ("ph", "core")
    placed = (
        P(pair, "col", None),
        P(pair, None),
        P(pair),
        P(pair, "col", None, None),
        P(pair, "col"),
        P(pair),
        P(pair),
    )
    return jax.shard_map(
        per_device,
        mesh=split,
        in_specs=placed,
        out_specs=(P(pair, "col", None), P(pair)),
        check_vma=False,
    )
```

```python
import functools

import jax
import jax.numpy as jnp
from jax import lax
from jax.experimental import pallas as pl
from jax.experimental.pallas import tpu as pltpu
from jax.sharding import PartitionSpec as P

COL_DEV = 8
SWEEPS = 3
PAIR_BLOCK = 8


def couple_kernel(slot_dev, links_ref, nlive_ref, tiles_ref, colamp_ref, out_ref):
    step = pl.program_id(0)
    width = tiles_ref.shape[-1]
    for q in range(PAIR_BLOCK):
        pair = step * PAIR_BLOCK + q
        live = nlive_ref[pair]
        lefts = []
        for m in range(slot_dev):
            block = colamp_ref[links_ref[pair * slot_dev + m]]
            left = jnp.dot(tiles_ref[q, m], block, preferred_element_type=jnp.float32)
            lefts.append(jnp.where(m < live, left, 0.0).astype(jnp.bfloat16))
        lcat = jnp.concatenate(lefts, axis=1)
        tcat = jnp.concatenate([tiles_ref[q, m] for m in range(slot_dev)], axis=1)
        acc = lax.dot_general(
            lcat, tcat, (((1,), (1,)), ((), ())), preferred_element_type=jnp.float32
        )
        out_ref[:, q] = acc.reshape(out_ref.shape[0], out_ref.shape[2], width).astype(out_ref.dtype)


def couple(tiles, colamp, links, nlive, col_size):
    pair_dev, slot_dev, width, _ = tiles.shape
    ncol = colamp.shape[0]
    rows = width // col_size
    grid_spec = pltpu.PrefetchScalarGridSpec(
        num_scalar_prefetch=2,
        grid=(pair_dev // PAIR_BLOCK,),
        in_specs=[
            pl.BlockSpec((PAIR_BLOCK, slot_dev, width, width), lambda i, *_: (i, 0, 0, 0)),
            pl.BlockSpec((ncol, width, width), lambda i, *_: (0, 0, 0)),
        ],
        out_specs=pl.BlockSpec(
            (col_size, PAIR_BLOCK, rows, width), lambda i, *_: (0, i, 0, 0)
        ),
    )
    flops = 4 * pair_dev * slot_dev * width**3
    return pl.pallas_call(
        functools.partial(couple_kernel, slot_dev),
        grid_spec=grid_spec,
        out_shape=jax.ShapeDtypeStruct((col_size, pair_dev, rows, width), jnp.float32),
        compiler_params=pltpu.CompilerParams(vmem_limit_bytes=48 * 1024 * 1024),
        cost_estimate=pl.CostEstimate(
            flops=flops,
            bytes_accessed=tiles.size * 2 + colamp.size * 2 + pair_dev * width * width * 4,
            transcendentals=0,
        ),
    )(links.reshape(-1), nlive, tiles, colamp)


def column_amplitudes(amplitudes, one_hot, pair_size, col_size):
    pair_dev, rows, width = amplitudes.shape
    ncol = one_hot.shape[0]
    contrib = jnp.dot(
        one_hot, amplitudes.reshape(pair_dev, rows * width), precision=lax.Precision.HIGHEST
    )
    per = ncol // pair_size
    parts = lax.all_to_all(contrib, ("core", "ph"), 0, 0, tiled=True)
    mine = jnp.sum(parts.reshape(pair_size, per, rows * width), axis=0)
    mine = mine.astype(jnp.bfloat16).reshape(1, per, rows, width)
    peers = pair_size // 2 * col_size
    sent = jnp.broadcast_to(mine, (peers, per, rows, width))
    got = lax.all_to_all(sent, ("ph", "col"), 0, 0, tiled=True)
    other = lax.ppermute(got, "core", [(0, 1), (1, 0)])
    both = jnp.stack([got, other]).reshape(2, pair_size // 2, col_size, per, rows, width)
    return both.transpose(0, 1, 3, 2, 4, 5).reshape(ncol, col_size * rows, width)


def per_device(integrals, pno_energy, shift, intersections, links, counts, column_of):
    pair_dev = integrals.shape[0]
    row_count = integrals.shape[1]
    slot_dev = intersections.shape[1]
    col_size = lax.axis_size("col")
    pair_size = lax.axis_size("ph") * lax.axis_size("core")
    ncol_all = COL_DEV * col_size
    rank = lax.axis_index("col")
    row_energy = lax.dynamic_slice_in_dim(pno_energy, rank * row_count, row_count, 1)
    denom = row_energy[:, :, None] + pno_energy[:, None, :] + shift[:, None, None]
    kfloat = integrals.astype(jnp.float32)
    amplitudes = -kfloat / denom
    one_hot = (jnp.arange(ncol_all, dtype=jnp.int32)[:, None] == column_of[None, :]).astype(
        jnp.float32
    )
    nlive = jnp.clip(counts - rank * slot_dev, 0, slot_dev).astype(jnp.int32)
    local_links = (links + ncol_all // 2 * lax.axis_index("core")) % ncol_all
    blocks = [integrals]
    for k in range(1, col_size):
        ring = [(i, (i + k) % col_size) for i in range(col_size)]
        blocks.append(lax.ppermute(integrals, "col", ring))
    owner_of = (rank - jnp.arange(col_size)) % col_size
    full_energy = pno_energy.reshape(pair_dev, col_size, 1, row_count, 1)
    denom_full = full_energy + pno_energy[:, None, None, None, :] + shift[:, None, None, None, None]
    for sweep in range(SWEEPS):
        colamp = column_amplitudes(amplitudes, one_hot, pair_size, col_size)
        partial = couple(intersections, colamp, local_links, nlive, col_size)
        if sweep == 0:
            partial, blocks = lax.optimization_barrier((partial, blocks))
            k_full = jnp.take(jnp.stack(blocks), owner_of, axis=0).astype(jnp.float32)
            weight = k_full / jnp.swapaxes(denom_full[:, :, 0], 0, 1)
        if sweep < SWEEPS - 1:
            parts = lax.all_to_all(partial, "col", 0, 0, tiled=True)
            coupled = jnp.sum(parts, axis=0)
        else:
            share = -jnp.sum(weight * partial, axis=(0, 2, 3))
            extra = jnp.zeros((row_count, partial.shape[-1]), jnp.float32)
            extra = extra.at[0, :pair_dev].set(share)
            extra = jnp.broadcast_to(extra, (col_size, 1) + extra.shape)
            parts = lax.all_to_all(jnp.concatenate([partial, extra], axis=1), "col", 0, 0, tiled=True)
            coupled = jnp.sum(parts[:, :pair_dev], axis=0)
            shares = parts[:, pair_dev, 0, :pair_dev]
        amplitudes = -(kfloat + coupled) / denom
    base = -jnp.sum(weight * k_full, axis=(0, 2, 3))
    pair_energy = base + jnp.sum(shares, axis=0)
    return (amplitudes, pair_energy)


def solution(mesh):
    col_size, pair_size = mesh.devices.shape
    split = jax.sharding.Mesh(
        mesh.devices.reshape(col_size, pair_size // 2, 2), ("col", "ph", "core")
    )
    pair = ("ph", "core")
    placed = (
        P(pair, "col", None),
        P(pair, None),
        P(pair),
        P(pair, "col", None, None),
        P(pair, "col"),
        P(pair),
        P(pair),
    )
    return jax.shard_map(
        per_device,
        mesh=split,
        in_specs=placed,
        out_specs=(P(pair, "col", None), P(pair)),
        check_vma=False,
    )
```

```python
import functools

import jax
import jax.numpy as jnp
from jax import lax
from jax.experimental import pallas as pl
from jax.experimental.pallas import tpu as pltpu
from jax.sharding import PartitionSpec as P

COL_DEV = 8
SWEEPS = 3
PAIR_BLOCK = 8


def couple_kernel(slot_dev, links_ref, nlive_ref, tiles_ref, colamp_ref, out_ref):
    step = pl.program_id(0)
    width = tiles_ref.shape[-1]
    for q in range(PAIR_BLOCK):
        pair = step * PAIR_BLOCK + q
        live = nlive_ref[pair]
        lefts = []
        for m in range(slot_dev):
            block = colamp_ref[links_ref[pair * slot_dev + m]]
            left = jnp.dot(tiles_ref[q, m], block, preferred_element_type=jnp.float32)
            lefts.append(jnp.where(m < live, left, 0.0).astype(jnp.bfloat16))
        lcat = jnp.concatenate(lefts, axis=1)
        tcat = jnp.concatenate([tiles_ref[q, m] for m in range(slot_dev)], axis=1)
        acc = lax.dot_general(
            lcat, tcat, (((1,), (1,)), ((), ())), preferred_element_type=jnp.float32
        )
        out_ref[:, q] = acc.reshape(out_ref.shape[0], out_ref.shape[2], width).astype(out_ref.dtype)


def couple(tiles, colamp, links, nlive, col_size):
    pair_dev, slot_dev, width, _ = tiles.shape
    ncol = colamp.shape[0]
    rows = width // col_size
    grid_spec = pltpu.PrefetchScalarGridSpec(
        num_scalar_prefetch=2,
        grid=(pair_dev // PAIR_BLOCK,),
        in_specs=[
            pl.BlockSpec((PAIR_BLOCK, slot_dev, width, width), lambda i, *_: (i, 0, 0, 0)),
            pl.BlockSpec((ncol, width, width), lambda i, *_: (0, 0, 0)),
        ],
        out_specs=pl.BlockSpec(
            (col_size, PAIR_BLOCK, rows, width), lambda i, *_: (0, i, 0, 0)
        ),
    )
    flops = 4 * pair_dev * slot_dev * width**3
    return pl.pallas_call(
        functools.partial(couple_kernel, slot_dev),
        grid_spec=grid_spec,
        out_shape=jax.ShapeDtypeStruct((col_size, pair_dev, rows, width), jnp.float32),
        compiler_params=pltpu.CompilerParams(vmem_limit_bytes=48 * 1024 * 1024),
        cost_estimate=pl.CostEstimate(
            flops=flops,
            bytes_accessed=tiles.size * 2 + colamp.size * 2 + pair_dev * width * width * 4,
            transcendentals=0,
        ),
    )(links.reshape(-1), nlive, tiles, colamp)


def column_amplitudes(amplitudes, one_hot, pair_size, col_size):
    pair_dev, rows, width = amplitudes.shape
    ncol = one_hot.shape[0]
    contrib = jnp.dot(
        one_hot, amplitudes.reshape(pair_dev, rows * width), precision=lax.Precision.HIGHEST
    )
    per = ncol // pair_size
    parts = lax.all_to_all(contrib, ("core", "ph"), 0, 0, tiled=True)
    mine = jnp.sum(parts.reshape(pair_size, per, rows * width), axis=0)
    mine = mine.astype(jnp.bfloat16).reshape(1, per, rows, width)
    peers = pair_size // 2 * col_size
    sent = jnp.broadcast_to(mine, (peers, per, rows, width))
    got = lax.all_to_all(sent, ("ph", "col"), 0, 0, tiled=True)
    other = lax.ppermute(got, "core", [(0, 1), (1, 0)])
    both = jnp.stack([got, other]).reshape(2, pair_size // 2, col_size, per, rows, width)
    return both.transpose(0, 1, 3, 2, 4, 5).reshape(ncol, col_size * rows, width)


def per_device(integrals, pno_energy, shift, intersections, links, counts, column_of):
    pair_dev = integrals.shape[0]
    row_count = integrals.shape[1]
    slot_dev = intersections.shape[1]
    col_size = lax.axis_size("col")
    pair_size = lax.axis_size("ph") * lax.axis_size("core")
    ncol_all = COL_DEV * col_size
    rank = lax.axis_index("col")
    row_energy = lax.dynamic_slice_in_dim(pno_energy, rank * row_count, row_count, 1)
    denom = row_energy[:, :, None] + pno_energy[:, None, :] + shift[:, None, None]
    kfloat = integrals.astype(jnp.float32)
    amplitudes = -kfloat / denom
    one_hot = (jnp.arange(ncol_all, dtype=jnp.int32)[:, None] == column_of[None, :]).astype(
        jnp.float32
    )
    nlive = jnp.clip(counts - rank * slot_dev, 0, slot_dev).astype(jnp.int32)
    local_links = (links + ncol_all // 2 * lax.axis_index("core")) % ncol_all
    held = integrals[None]
    bit = 1
    while bit < col_size:
        flip = [(i, i ^ bit) for i in range(col_size)]
        held = jnp.concatenate([held, lax.ppermute(held, "col", flip)], axis=0)
        bit *= 2
    blocks = held
    owner_of = rank ^ jnp.arange(col_size)
    full_energy = pno_energy.reshape(pair_dev, col_size, 1, row_count, 1)
    denom_full = full_energy + pno_energy[:, None, None, None, :] + shift[:, None, None, None, None]
    for sweep in range(SWEEPS):
        colamp = column_amplitudes(amplitudes, one_hot, pair_size, col_size)
        partial = couple(intersections, colamp, local_links, nlive, col_size)
        if sweep == 0:
            partial, blocks = lax.optimization_barrier((partial, blocks))
            k_full = jnp.take(blocks, owner_of, axis=0).astype(jnp.float32)
            weight = k_full / jnp.swapaxes(denom_full[:, :, 0], 0, 1)
        if sweep < SWEEPS - 1:
            parts = lax.all_to_all(partial, "col", 0, 0, tiled=True)
            coupled = jnp.sum(parts, axis=0)
        else:
            share = -jnp.sum(weight * partial, axis=(0, 2, 3))
            extra = jnp.zeros((row_count, partial.shape[-1]), jnp.float32)
            extra = extra.at[0, :pair_dev].set(share)
            extra = jnp.broadcast_to(extra, (col_size, 1) + extra.shape)
            parts = lax.all_to_all(jnp.concatenate([partial, extra], axis=1), "col", 0, 0, tiled=True)
            coupled = jnp.sum(parts[:, :pair_dev], axis=0)
            shares = parts[:, pair_dev, 0, :pair_dev]
        amplitudes = -(kfloat + coupled) / denom
    base = -jnp.sum(weight * k_full, axis=(0, 2, 3))
    pair_energy = base + jnp.sum(shares, axis=0)
    return (amplitudes, pair_energy)


def solution(mesh):
    col_size, pair_size = mesh.devices.shape
    split = jax.sharding.Mesh(
        mesh.devices.reshape(col_size, pair_size // 2, 2), ("col", "ph", "core")
    )
    pair = ("ph", "core")
    placed = (
        P(pair, "col", None),
        P(pair, None),
        P(pair),
        P(pair, "col", None, None),
        P(pair, "col"),
        P(pair),
        P(pair),
    )
    return jax.shard_map(
        per_device,
        mesh=split,
        in_specs=placed,
        out_specs=(P(pair, "col", None), P(pair)),
        check_vma=False,
    )
```

```python
import functools

import jax
import jax.numpy as jnp
from jax import lax
from jax.experimental import pallas as pl
from jax.experimental.pallas import tpu as pltpu
from jax.sharding import PartitionSpec as P

COL_DEV = 8
SWEEPS = 3
PAIR_BLOCK = 8


def couple_kernel(slot_dev, links_ref, nlive_ref, tiles_ref, colamp_ref, out_ref):
    step = pl.program_id(0)
    width = tiles_ref.shape[-1]
    for q in range(PAIR_BLOCK):
        pair = step * PAIR_BLOCK + q
        live = nlive_ref[pair]
        lefts = []
        for m in range(slot_dev):
            block = colamp_ref[links_ref[pair * slot_dev + m]]
            left = jnp.dot(tiles_ref[q, m], block, preferred_element_type=jnp.float32)
            lefts.append(jnp.where(m < live, left, 0.0).astype(jnp.bfloat16))
        lcat = jnp.concatenate(lefts, axis=1)
        tcat = jnp.concatenate([tiles_ref[q, m] for m in range(slot_dev)], axis=1)
        acc = lax.dot_general(
            lcat, tcat, (((1,), (1,)), ((), ())), preferred_element_type=jnp.float32
        )
        out_ref[:, q] = acc.reshape(out_ref.shape[0], out_ref.shape[2], width).astype(out_ref.dtype)


def couple(tiles, colamp, links, nlive, col_size):
    pair_dev, slot_dev, width, _ = tiles.shape
    ncol = colamp.shape[0]
    rows = width // col_size
    grid_spec = pltpu.PrefetchScalarGridSpec(
        num_scalar_prefetch=2,
        grid=(pair_dev // PAIR_BLOCK,),
        in_specs=[
            pl.BlockSpec((PAIR_BLOCK, slot_dev, width, width), lambda i, *_: (i, 0, 0, 0)),
            pl.BlockSpec((ncol, width, width), lambda i, *_: (0, 0, 0)),
        ],
        out_specs=pl.BlockSpec(
            (col_size, PAIR_BLOCK, rows, width), lambda i, *_: (0, i, 0, 0)
        ),
    )
    flops = 4 * pair_dev * slot_dev * width**3
    return pl.pallas_call(
        functools.partial(couple_kernel, slot_dev),
        grid_spec=grid_spec,
        out_shape=jax.ShapeDtypeStruct((col_size, pair_dev, rows, width), jnp.float32),
        compiler_params=pltpu.CompilerParams(vmem_limit_bytes=48 * 1024 * 1024),
        cost_estimate=pl.CostEstimate(
            flops=flops,
            bytes_accessed=tiles.size * 2 + colamp.size * 2 + pair_dev * width * width * 4,
            transcendentals=0,
        ),
    )(links.reshape(-1), nlive, tiles, colamp)


def column_amplitudes(amplitudes, one_hot, pair_size, col_size):
    pair_dev, rows, width = amplitudes.shape
    ncol = one_hot.shape[0]
    contrib = jnp.dot(
        one_hot, amplitudes.reshape(pair_dev, rows * width), precision=lax.Precision.HIGHEST
    )
    per = ncol // pair_size
    parts = lax.all_to_all(contrib, ("core", "ph"), 0, 0, tiled=True)
    mine = jnp.sum(parts.reshape(pair_size, per, rows * width), axis=0)
    mine = mine.astype(jnp.bfloat16).reshape(1, per, rows, width)
    peers = pair_size // 2 * col_size
    sent = jnp.broadcast_to(mine, (peers, per, rows, width))
    got = lax.all_to_all(sent, ("ph", "col"), 0, 0, tiled=True)
    other = lax.ppermute(got, "core", [(0, 1), (1, 0)])
    both = jnp.stack([got, other]).reshape(2, pair_size // 2, col_size, per, rows, width)
    return both.transpose(0, 1, 3, 2, 4, 5).reshape(ncol, col_size * rows, width)


def per_device(integrals, pno_energy, shift, intersections, links, counts, column_of):
    pair_dev = integrals.shape[0]
    row_count = integrals.shape[1]
    slot_dev = intersections.shape[1]
    col_size = lax.axis_size("col")
    pair_size = lax.axis_size("ph") * lax.axis_size("core")
    ncol_all = COL_DEV * col_size
    rank = lax.axis_index("col")
    row_energy = lax.dynamic_slice_in_dim(pno_energy, rank * row_count, row_count, 1)
    denom = row_energy[:, :, None] + pno_energy[:, None, :] + shift[:, None, None]
    kfloat = integrals.astype(jnp.float32)
    amplitudes = -kfloat / denom
    one_hot = (jnp.arange(ncol_all, dtype=jnp.int32)[:, None] == column_of[None, :]).astype(
        jnp.float32
    )
    nlive = jnp.clip(counts - rank * slot_dev, 0, slot_dev).astype(jnp.int32)
    local_links = (links + ncol_all // 2 * lax.axis_index("core")) % ncol_all
    blocks = [integrals]
    for k in range(1, col_size):
        ring = [(i, (i + k) % col_size) for i in range(col_size)]
        blocks.append(lax.ppermute(integrals, "col", ring))
    owner_of = (rank - jnp.arange(col_size)) % col_size
    full_energy = pno_energy.reshape(pair_dev, col_size, 1, row_count, 1)
    denom_full = full_energy + pno_energy[:, None, None, None, :] + shift[:, None, None, None, None]
    for sweep in range(SWEEPS):
        colamp = column_amplitudes(amplitudes, one_hot, pair_size, col_size)
        partial = couple(intersections, colamp, local_links, nlive, col_size)
        if sweep == 0:
            partial, blocks = lax.optimization_barrier((partial, blocks))
            k_full = jnp.take(jnp.stack(blocks), owner_of, axis=0).astype(jnp.float32)
            weight = k_full / jnp.swapaxes(denom_full[:, :, 0], 0, 1)
        if sweep < SWEEPS - 1:
            coupled = jnp.take(partial, rank, axis=0)
            for k in range(1, col_size):
                ring = [(i, (i + k) % col_size) for i in range(col_size)]
                piece = jnp.take(partial, (rank + k) % col_size, axis=0)
                coupled = coupled + lax.ppermute(piece, "col", ring)
        else:
            share = -jnp.sum(weight * partial, axis=(0, 2, 3))
            extra = jnp.zeros((row_count, partial.shape[-1]), jnp.float32)
            extra = extra.at[0, :pair_dev].set(share)
            extra = jnp.broadcast_to(extra, (col_size, 1) + extra.shape)
            parts = lax.all_to_all(jnp.concatenate([partial, extra], axis=1), "col", 0, 0, tiled=True)
            coupled = jnp.sum(parts[:, :pair_dev], axis=0)
            shares = parts[:, pair_dev, 0, :pair_dev]
        amplitudes = -(kfloat + coupled) / denom
    base = -jnp.sum(weight * k_full, axis=(0, 2, 3))
    pair_energy = base + jnp.sum(shares, axis=0)
    return (amplitudes, pair_energy)


def solution(mesh):
    col_size, pair_size = mesh.devices.shape
    split = jax.sharding.Mesh(
        mesh.devices.reshape(col_size, pair_size // 2, 2), ("col", "ph", "core")
    )
    pair = ("ph", "core")
    placed = (
        P(pair, "col", None),
        P(pair, None),
        P(pair),
        P(pair, "col", None, None),
        P(pair, "col"),
        P(pair),
        P(pair),
    )
    return jax.shard_map(
        per_device,
        mesh=split,
        in_specs=placed,
        out_specs=(P(pair, "col", None), P(pair)),
        check_vma=False,
    )
```

```python
import functools

import jax
import jax.numpy as jnp
from jax import lax
from jax.experimental import pallas as pl
from jax.experimental.pallas import tpu as pltpu
from jax.sharding import PartitionSpec as P

COL_DEV = 8
SWEEPS = 3
PAIR_BLOCK = 8


def couple_kernel(slot_dev, links_ref, nlive_ref, tiles_ref, colamp_ref, out_ref):
    step = pl.program_id(0)
    width = tiles_ref.shape[-1]
    for q in range(PAIR_BLOCK):
        pair = step * PAIR_BLOCK + q
        live = nlive_ref[pair]
        lefts = []
        for m in range(slot_dev):
            block = colamp_ref[links_ref[pair * slot_dev + m]]
            left = jnp.dot(tiles_ref[q, m], block, preferred_element_type=jnp.float32)
            lefts.append(jnp.where(m < live, left, 0.0).astype(jnp.bfloat16))
        lcat = jnp.concatenate(lefts, axis=1)
        tcat = jnp.concatenate([tiles_ref[q, m] for m in range(slot_dev)], axis=1)
        acc = lax.dot_general(
            lcat, tcat, (((1,), (1,)), ((), ())), preferred_element_type=jnp.float32
        )
        out_ref[:, q] = acc.reshape(out_ref.shape[0], out_ref.shape[2], width).astype(out_ref.dtype)


def couple(tiles, colamp, links, nlive, col_size):
    pair_dev, slot_dev, width, _ = tiles.shape
    ncol = colamp.shape[0]
    rows = width // col_size
    grid_spec = pltpu.PrefetchScalarGridSpec(
        num_scalar_prefetch=2,
        grid=(pair_dev // PAIR_BLOCK,),
        in_specs=[
            pl.BlockSpec((PAIR_BLOCK, slot_dev, width, width), lambda i, *_: (i, 0, 0, 0)),
            pl.BlockSpec((ncol, width, width), lambda i, *_: (0, 0, 0)),
        ],
        out_specs=pl.BlockSpec(
            (col_size, PAIR_BLOCK, rows, width), lambda i, *_: (0, i, 0, 0)
        ),
    )
    flops = 4 * pair_dev * slot_dev * width**3
    return pl.pallas_call(
        functools.partial(couple_kernel, slot_dev),
        grid_spec=grid_spec,
        out_shape=jax.ShapeDtypeStruct((col_size, pair_dev, rows, width), jnp.float32),
        compiler_params=pltpu.CompilerParams(vmem_limit_bytes=48 * 1024 * 1024),
        cost_estimate=pl.CostEstimate(
            flops=flops,
            bytes_accessed=tiles.size * 2 + colamp.size * 2 + pair_dev * width * width * 4,
            transcendentals=0,
        ),
    )(links.reshape(-1), nlive, tiles, colamp)


def column_amplitudes(amplitudes, one_hot, pair_size, col_size):
    pair_dev, rows, width = amplitudes.shape
    ncol = one_hot.shape[0]
    contrib = jnp.dot(
        one_hot, amplitudes.reshape(pair_dev, rows * width), precision=lax.Precision.HIGHEST
    )
    per = ncol // pair_size
    parts = lax.all_to_all(contrib, ("core", "ph"), 0, 0, tiled=True)
    mine = jnp.sum(parts.reshape(pair_size, per, rows * width), axis=0)
    mine = mine.astype(jnp.bfloat16).reshape(1, per, rows, width)
    peers = pair_size // 2 * col_size
    sent = jnp.broadcast_to(mine, (peers, per, rows, width))
    got = lax.all_to_all(sent, ("ph", "col"), 0, 0, tiled=True)
    other = lax.ppermute(got, "core", [(0, 1), (1, 0)])
    both = jnp.stack([got, other]).reshape(2, pair_size // 2, col_size, per, rows, width)
    return both.transpose(0, 1, 3, 2, 4, 5).reshape(ncol, col_size * rows, width)


def per_device(integrals, pno_energy, shift, intersections, links, counts, column_of):
    pair_dev = integrals.shape[0]
    row_count = integrals.shape[1]
    slot_dev = intersections.shape[1]
    col_size = lax.axis_size("col")
    pair_size = lax.axis_size("ph") * lax.axis_size("core")
    ncol_all = COL_DEV * col_size
    rank = lax.axis_index("col")
    row_energy = lax.dynamic_slice_in_dim(pno_energy, rank * row_count, row_count, 1)
    denom = row_energy[:, :, None] + pno_energy[:, None, :] + shift[:, None, None]
    kfloat = integrals.astype(jnp.float32)
    amplitudes = -kfloat / denom
    one_hot = (jnp.arange(ncol_all, dtype=jnp.int32)[:, None] == column_of[None, :]).astype(
        jnp.float32
    )
    nlive = jnp.clip(counts - rank * slot_dev, 0, slot_dev).astype(jnp.int32)
    local_links = (links + ncol_all // 2 * lax.axis_index("core")) % ncol_all
    blocks = [integrals]
    for k in range(1, col_size):
        ring = [(i, (i + k) % col_size) for i in range(col_size)]
        blocks.append(lax.ppermute(integrals, "col", ring))
    owner_of = (rank - jnp.arange(col_size)) % col_size
    full_energy = pno_energy.reshape(pair_dev, col_size, 1, row_count, 1)
    denom_full = full_energy + pno_energy[:, None, None, None, :] + shift[:, None, None, None, None]
    for sweep in range(SWEEPS):
        colamp = column_amplitudes(amplitudes, one_hot, pair_size, col_size)
        partial = couple(intersections, colamp, local_links, nlive, col_size)
        if sweep == 1:
            partial, blocks = lax.optimization_barrier((partial, blocks))
            k_full = jnp.take(jnp.stack(blocks), owner_of, axis=0).astype(jnp.float32)
            weight = k_full / jnp.swapaxes(denom_full[:, :, 0], 0, 1)
        if sweep < SWEEPS - 1:
            parts = lax.all_to_all(partial, "col", 0, 0, tiled=True)
            coupled = jnp.sum(parts, axis=0)
        else:
            share = -jnp.sum(weight * partial, axis=(0, 2, 3))
            extra = jnp.zeros((row_count, partial.shape[-1]), jnp.float32)
            extra = extra.at[0, :pair_dev].set(share)
            extra = jnp.broadcast_to(extra, (col_size, 1) + extra.shape)
            parts = lax.all_to_all(jnp.concatenate([partial, extra], axis=1), "col", 0, 0, tiled=True)
            coupled = jnp.sum(parts[:, :pair_dev], axis=0)
            shares = parts[:, pair_dev, 0, :pair_dev]
        amplitudes = -(kfloat + coupled) / denom
    base = -jnp.sum(weight * k_full, axis=(0, 2, 3))
    pair_energy = base + jnp.sum(shares, axis=0)
    return (amplitudes, pair_energy)


def solution(mesh):
    col_size, pair_size = mesh.devices.shape
    split = jax.sharding.Mesh(
        mesh.devices.reshape(col_size, pair_size // 2, 2), ("col", "ph", "core")
    )
    pair = ("ph", "core")
    placed = (
        P(pair, "col", None),
        P(pair, None),
        P(pair),
        P(pair, "col", None, None),
        P(pair, "col"),
        P(pair),
        P(pair),
    )
    return jax.shard_map(
        per_device,
        mesh=split,
        in_specs=placed,
        out_specs=(P(pair, "col", None), P(pair)),
        check_vma=False,
    )
```
